128 devices in a mesh: page: 8 (over z, core), tensor: 16 (over x, y).
Axes of the slice: x: 4, y: 4, z: 4, core: 2. Of those that a mesh axis runs over, the one named last changes fastest.
Arguments:
- hidden_in: bfloat16 [1, 32, 8192], P(None, 'tensor', 'page'), may hold values from -6 to 6
- w_query: bfloat16 [8192, 8192], P('page', 'tensor'), may hold values from -0.0625 to 0.0625
- w_keyval: bfloat16 [8192, 2048], P('page', 'tensor'), may hold values from -0.0625 to 0.0625
- w_output: bfloat16 [8192, 8192], P('tensor', 'page'), may hold values from -0.0625 to 0.0625
- kv_pool: bfloat16 [8192, 64, 2048], P(('page', 'tensor'))
- page_table: int32 [8192], replicated, may hold values from 0 to 8191, each once
- selected: int32 [1, 32, 8, 32], replicated, may hold values from 0 to 255, as said below
Outputs:
- attn_out: bfloat16 [1, 32, 8192], P(None, 'tensor', 'page')
- new_kv: bfloat16 [1, 32, 2048], P(None, 'page', 'tensor')
The draws below stay inside these ranges and needn't reach their ends.
Inputs may be any that keep to these rules, and one draw needn't show every extreme that they name: `page_table`: each pool slot holds exactly one page: entry s * 256 + l is the slot of page l of sequence s. `selected`: the 32 pages of one row are different.
All inputs are finite; a program needn't handle non-finite values.
Results may differ from the reference program's by a relative error of at most 0.018.
The reference program's roundings to bfloat16 on the way count: a program that leaves them out, or rounds other values in their place, can miss the bound.
Values may be sent and summed in bfloat16 or wider, within the bound.
No kernel may reach another device: no remote copies, remote signals or barrier semaphores. Data moves between devices by JAX's collectives and lax.ppermute only.
A program may use at most 192 MiB of HBM per device.

```python
import math
import jax
import jax.numpy as jnp
from jax import lax

D = 8192
H = 64
KVH = 8
HD = 128
PAGE_TOK = 64
NSEL = 32
STEPS = 1
PAGES = 256
SEQS = 32
POOL = 8192


def draw_selected(key, part):
    scores = jax.random.randint(key, (STEPS, SEQS, KVH, PAGES), 0, 4096, dtype=jnp.int32) * PAGES + jnp.arange(PAGES, dtype=jnp.int32)
    return lax.top_k(scores, NSEL)[1].astype(jnp.int32)


def draw_kv_pool(key, part):
    shape_five = (POOL, PAGE_TOK, KVH, 2, HD)
    base_vals = jnp.clip(jax.random.normal(jax.random.fold_in(key, 11), shape_five, jnp.float32), -6.0, 6.0)
    kind_scale = jnp.array([0.3, 1.0], jnp.float32).reshape(1, 1, 1, 2, 1)
    result = base_vals * kind_scale
    return result.reshape(POOL, PAGE_TOK, 2 * KVH * HD).astype(jnp.bfloat16)


def block_scale(key, shape, cuts, low, largest):
    level = 1.0
    for dim, blocks in cuts:
        draws = jax.random.uniform(jax.random.fold_in(jax.random.fold_in(key, 6), dim), (blocks,), jnp.float32, low / len(cuts), largest / len(cuts))
        level = level * jnp.repeat(jnp.exp(draws), shape[dim] // blocks).reshape((-1,) + (1,) * (len(shape) - 1 - dim))
    return level


def gaussian(rng, dims, width, most, cuts=(), held_as=jnp.bfloat16):
    values = width * jax.random.normal(rng, dims, jnp.float32)
    if cuts:
        values = values * block_scale(rng, dims, cuts, -0.22, 0.18)
    return jnp.clip(values, -most, most).astype(held_as)


def setup_inputs(seed: int = 0) -> dict:
    keys = jax.random.split(jax.random.key(seed), 8)
    return {
        "hidden_in": gaussian(keys[0], (STEPS, SEQS, D), 1.0, 6.0, ((1, 16), (2, 8))),
        "w_query": gaussian(keys[1], (D, H * HD), D ** -0.5, 0.0625, ((0, 8), (1, 16))),
        "w_keyval": gaussian(keys[2], (D, 2 * KVH * HD), D ** -0.5, 0.0625, ((0, 8), (1, 16))),
        "w_output": gaussian(keys[3], (H * HD, D), (H * HD) ** -0.5, 0.0625, ((0, 16), (1, 8))),
        "kv_pool": draw_kv_pool(jax.random.fold_in(keys[7], 71), 0),
        "page_table": jax.random.permutation(keys[5], POOL).astype(jnp.int32),
        "selected": draw_selected(jax.random.fold_in(keys[7], 71), 0),
    }


def frequencies(head_dim):
    half_dim = head_dim // 2
    index = jnp.arange(half_dim, dtype=jnp.float32)
    base_freq = jnp.exp(-(2.0 * index / head_dim) * math.log(500000.0))
    wavelen = 2.0 * math.pi / base_freq
    smooth = (8192.0 / wavelen - 1.0) / 3.0
    middle = (1.0 - smooth) * base_freq / 8.0 + smooth * base_freq
    scaled = jnp.where(wavelen > 8192.0, base_freq / 8.0, base_freq)
    is_middle = jnp.logical_and(wavelen >= 2048.0, wavelen <= 8192.0)
    return jnp.where(is_middle, middle, scaled)

def rotate(vectors, position):
    half_dim = vectors.shape[-1] // 2
    angles = position * frequencies(vectors.shape[-1])
    cosine = jnp.cos(angles)
    sine_v = jnp.sin(angles)
    first_half = vectors[..., :half_dim]
    second_half = vectors[..., half_dim:]
    return jnp.concatenate([first_half * cosine - second_half * sine_v, first_half * sine_v + second_half * cosine], axis=-1)

def reference(hidden_in, w_query, w_keyval, w_output, kv_pool, page_table, selected):
    groups = H // KVH
    scale = 1.0 / math.sqrt(HD)
    pool_five = kv_pool.reshape(POOL, PAGE_TOK, KVH, 2, HD)
    head_ids = jnp.arange(KVH, dtype=jnp.int32)[:, None]
    outputs = []
    new_rows = []
    for step_no in range(STEPS):
        position = float(PAGES * PAGE_TOK + step_no)
        tok_rows = hidden_in[step_no]
        query = jnp.dot(tok_rows, w_query, preferred_element_type=jnp.float32).reshape(SEQS, H, HD)
        query = rotate(query, position).astype(jnp.bfloat16)
        keyval = jnp.dot(tok_rows, w_keyval, preferred_element_type=jnp.float32).reshape(SEQS, KVH, 2, HD)
        new_key = rotate(keyval[:, :, 0], position)
        new_rows.append(jnp.stack([new_key, keyval[:, :, 1]], axis=2).reshape(SEQS, 2 * KVH * HD).astype(jnp.bfloat16))

        def one_seq(packed):
            seq_query, seq_sel, seq_id = packed
            slot_ids = jnp.take(page_table, seq_id * PAGES + seq_sel).astype(jnp.int32)
            gathered = pool_five[slot_ids, :, head_ids]
            key_rows = gathered[..., 0, :].astype(jnp.float32)
            val_rows = gathered[..., 1, :].astype(jnp.float32)
            grouped = seq_query.reshape(KVH, groups, HD).astype(jnp.float32)
            scores = jnp.einsum('ghd,gntd->ghnt', grouped, key_rows) * scale
            page_max = lax.optimization_barrier(jnp.max(scores, axis=-1))
            weights = jnp.exp(scores - page_max[..., None]).astype(jnp.bfloat16)
            page_total = lax.optimization_barrier(jnp.sum(weights.astype(jnp.float32), axis=-1))
            page_acc = jnp.einsum('ghnt,gntd->ghnd', weights.astype(jnp.float32), val_rows)
            top_max = lax.optimization_barrier(jnp.max(page_max, axis=-1))
            factor = jnp.exp(page_max - top_max[..., None])
            summed_total = lax.optimization_barrier(jnp.sum(page_total * factor, axis=-1))
            summed_acc = lax.optimization_barrier(jnp.sum(page_acc * factor[..., None], axis=2))
            return (summed_acc / summed_total[..., None]).reshape(H, HD).astype(jnp.bfloat16)
        heads = lax.map(one_seq, (query, selected[step_no], jnp.arange(SEQS, dtype=jnp.int32)))
        outputs.append(jnp.dot(heads.reshape(SEQS, H * HD), w_output, preferred_element_type=jnp.float32).astype(jnp.bfloat16))
    return (jnp.stack(outputs), jnp.stack(new_rows))
```

```python
import math

import jax
import jax.numpy as jnp
from jax import lax
from jax.sharding import PartitionSpec as P

H = 64
KVH = 8
HD = 128
PAGE_TOK = 64
PAGES = 256


NEG_BIG = -1e30


def frequencies(head_dim):
    half_dim = head_dim // 2
    index = jnp.arange(half_dim, dtype=jnp.float32)
    base_freq = jnp.exp(-(2.0 * index / head_dim) * math.log(500000.0))
    wavelen = 2.0 * math.pi / base_freq
    smooth = (8192.0 / wavelen - 1.0) / 3.0
    middle = (1.0 - smooth) * base_freq / 8.0 + smooth * base_freq
    scaled = jnp.where(wavelen > 8192.0, base_freq / 8.0, base_freq)
    is_middle = jnp.logical_and(wavelen >= 2048.0, wavelen <= 8192.0)
    return jnp.where(is_middle, middle, scaled)


def rotate(vectors, position):
    half_dim = vectors.shape[-1] // 2
    angles = position * frequencies(vectors.shape[-1])
    cosine = jnp.cos(angles)
    sine_v = jnp.sin(angles)
    first_half = vectors[..., :half_dim]
    second_half = vectors[..., half_dim:]
    return jnp.concatenate(
        [first_half * cosine - second_half * sine_v, first_half * sine_v + second_half * cosine],
        axis=-1,
    )


def gather_blocks(x, axis, n):
    return lax.all_to_all(jnp.broadcast_to(x[None], (n,) + x.shape), axis, 0, 0, tiled=True)


def butterfly_sum(x, axis, n):
    d = 1
    while d < n:
        x = x + lax.ppermute(x, axis, [(i, i ^ d) for i in range(n)])
        d *= 2
    return x


def per_device(hidden_in, w_query, w_keyval, w_output, kv_pool, page_table, selected):
    n_page = lax.axis_size("page")
    n_tensor = lax.axis_size("tensor")
    my_page = lax.axis_index("page")
    my_tensor = lax.axis_index("tensor")
    seqs = selected.shape[1]
    groups = H // KVH
    local_heads = H // n_tensor
    scale = 1.0 / math.sqrt(HD)
    slots = kv_pool.shape[0]
    pool_size = page_table.shape[0]
    device = my_page * n_tensor + my_tensor
    position = float(PAGES * PAGE_TOK)
    seq_share = seqs // n_page
    query_cols = w_query.shape[1]
    sub_heads = w_keyval.shape[1] // HD

    my_slots = device * slots + jnp.arange(slots, dtype=jnp.int32)
    match = page_table[None, :] == my_slots[:, None]
    my_logical = jnp.sum(
        jnp.where(match, jnp.arange(pool_size, dtype=jnp.int32)[None, :], 0), axis=1
    )
    seq_of = my_logical // PAGES
    page_of = my_logical % PAGES
    sel_rows = selected[0][seq_of]
    picked = jnp.any(sel_rows == page_of[:, None, None], axis=2)

    tok_all = gather_blocks(hidden_in[0], "tensor", n_tensor).reshape(seqs, -1)
    part_q = jnp.dot(tok_all, w_query, preferred_element_type=jnp.float32)
    part_kv = jnp.dot(tok_all, w_keyval, preferred_element_type=jnp.float32)
    summed = butterfly_sum(jnp.concatenate([part_q, part_kv], axis=1), "page", n_page)
    query = rotate(summed[:, :query_cols].reshape(seqs, local_heads, HD), position)
    query = query.astype(jnp.bfloat16).reshape(seqs, query_cols)
    keyval = summed[:, query_cols:].reshape(seqs, sub_heads, HD)
    kind_ids = (my_tensor * sub_heads + jnp.arange(sub_heads, dtype=jnp.int32)) % 2
    keyval = jnp.where(kind_ids[None, :, None] == 0, rotate(keyval, position), keyval)
    keyval = keyval.reshape(seqs, -1).astype(jnp.bfloat16)
    new_rows = lax.dynamic_slice_in_dim(keyval, my_page * seq_share, seq_share, 0)

    q_all = gather_blocks(query, "tensor", n_tensor)
    q_all = q_all.reshape(KVH, n_tensor // KVH, seqs, local_heads, HD)
    q_all = q_all.transpose(2, 0, 1, 3, 4).reshape(seqs, KVH, groups, HD)
    slot_query = q_all[seq_of]

    maxes, totals, accs = [], [], []
    for g in range(KVH):
        base = g * 2 * HD
        key_g = kv_pool[:, :, base:base + HD]
        val_g = kv_pool[:, :, base + HD:base + 2 * HD]
        sc = jnp.einsum(
            "shd,std->sht", slot_query[:, g], key_g, preferred_element_type=jnp.float32
        ) * scale
        pm = jnp.max(sc, axis=-1)
        wt = jnp.exp(sc - pm[..., None]).astype(jnp.bfloat16)
        pt = jnp.sum(wt.astype(jnp.float32), axis=-1)
        pa = jnp.einsum("sht,std->shd", wt, val_g, preferred_element_type=jnp.float32)
        maxes.append(pm)
        totals.append(pt)
        accs.append(pa)
    page_max = jnp.stack(maxes, axis=1)
    page_total = jnp.stack(totals, axis=1)
    page_acc = jnp.stack(accs, axis=1)
    pick = picked[:, :, None]
    page_max = jnp.where(pick, page_max, NEG_BIG).reshape(slots, H)
    page_total = jnp.where(pick, page_total, 0.0).reshape(slots, H)
    page_acc = jnp.where(pick[..., None], page_acc, 0.0).reshape(slots, H, HD)

    owner_rows = jnp.arange(seqs, dtype=jnp.int32)[:, None] == seq_of[None, :]
    owner_hot = owner_rows.astype(jnp.float32)
    loc_max = jnp.max(jnp.where(owner_rows[:, :, None], page_max[None], NEG_BIG), axis=1)
    factor = jnp.exp(page_max - loc_max[seq_of])
    loc_total = jnp.dot(owner_hot, page_total * factor, precision=lax.Precision.HIGHEST)
    loc_acc = jnp.dot(
        owner_hot,
        (page_acc * factor[..., None]).reshape(slots, H * HD),
        precision=lax.Precision.HIGHEST,
    ).reshape(seqs, H, HD)

    packed = jnp.concatenate([loc_acc, loc_total[..., None], loc_max[..., None]], axis=-1)
    width = HD + 2
    packed = packed.reshape(n_page, seq_share, n_tensor, local_heads, width)
    packed = packed.transpose(0, 2, 1, 3, 4).reshape(n_page * n_tensor, -1)
    got = lax.all_to_all(packed, ("page", "tensor"), 0, 0, tiled=True)
    got = got.reshape(n_page * n_tensor, seq_share, local_heads, width)
    src_max = got[..., HD + 1]
    top_max = jnp.max(src_max, axis=0)
    rescale = jnp.exp(src_max - top_max[None])
    full_total = jnp.sum(got[..., HD] * rescale, axis=0)
    full_acc = jnp.sum(got[..., :HD] * rescale[..., None], axis=0)
    heads = (full_acc / full_total[..., None]).astype(jnp.bfloat16)

    heads_all = gather_blocks(heads.reshape(seq_share, local_heads * HD), "page", n_page)
    heads_all = heads_all.reshape(seqs, local_heads * HD)
    part_out = jnp.dot(heads_all, w_output, preferred_element_type=jnp.float32)
    part_out = part_out.reshape(n_tensor, seqs // n_tensor, -1)
    out = jnp.sum(lax.all_to_all(part_out, "tensor", 0, 0, tiled=True), axis=0)
    return (out.astype(jnp.bfloat16)[None], new_rows[None])


def solution(mesh):
    return jax.shard_map(
        per_device,
        mesh=mesh,
        in_specs=(
            P(None, "tensor", "page"),
            P("page", "tensor"),
            P("page", "tensor"),
            P("tensor", "page"),
            P(("page", "tensor"), None, None),
            P(),
            P(),
        ),
        out_specs=(P(None, "tensor", "page"), P(None, "page", "tensor")),
        check_vma=False,
    )
```

```python
import math

import jax
import jax.numpy as jnp
from jax import lax
from jax.experimental import pallas as pl
from jax.sharding import PartitionSpec as P

H = 64
KVH = 8
HD = 128
PAGE_TOK = 64
PAGES = 256


NEG_BIG = -1e30


def frequencies(head_dim):
    half_dim = head_dim // 2
    index = jnp.arange(half_dim, dtype=jnp.float32)
    base_freq = jnp.exp(-(2.0 * index / head_dim) * math.log(500000.0))
    wavelen = 2.0 * math.pi / base_freq
    smooth = (8192.0 / wavelen - 1.0) / 3.0
    middle = (1.0 - smooth) * base_freq / 8.0 + smooth * base_freq
    scaled = jnp.where(wavelen > 8192.0, base_freq / 8.0, base_freq)
    is_middle = jnp.logical_and(wavelen >= 2048.0, wavelen <= 8192.0)
    return jnp.where(is_middle, middle, scaled)


def rotate(vectors, position):
    half_dim = vectors.shape[-1] // 2
    angles = position * frequencies(vectors.shape[-1])
    cosine = jnp.cos(angles)
    sine_v = jnp.sin(angles)
    first_half = vectors[..., :half_dim]
    second_half = vectors[..., half_dim:]
    return jnp.concatenate(
        [first_half * cosine - second_half * sine_v, first_half * sine_v + second_half * cosine],
        axis=-1,
    )


def gather_blocks(x, axis, n):
    return lax.all_to_all(jnp.broadcast_to(x[None], (n,) + x.shape), axis, 0, 0, tiled=True)


def butterfly_sum(x, axis, n):
    d = 1
    while d < n:
        x = x + lax.ppermute(x, axis, [(i, i ^ d) for i in range(n)])
        d *= 2
    return x


def attn_kernel(q_ref, kv_ref, acc_ref, m_ref, t_ref):
    tok = kv_ref.shape[1]
    rows = lax.broadcasted_iota(jnp.int32, (H, KVH * tok), 0) // (H // KVH)
    cols = lax.broadcasted_iota(jnp.int32, (H, KVH * tok), 1) // tok
    same_group = rows == cols
    scale = 1.0 / math.sqrt(HD)

    def body(j, carry):
        keys = jnp.concatenate(
            [kv_ref[j, :, pl.ds(g * 2 * HD, HD)] for g in range(KVH)], axis=0
        )
        vals = jnp.concatenate(
            [kv_ref[j, :, pl.ds(g * 2 * HD + HD, HD)] for g in range(KVH)], axis=0
        )
        sc = lax.dot_general(
            q_ref[j], keys, (((1,), (1,)), ((), ())), preferred_element_type=jnp.float32
        ) * scale
        sc = jnp.where(same_group, sc, -jnp.inf)
        pm = jnp.max(sc, axis=1, keepdims=True)
        wt = jnp.exp(sc - pm).astype(jnp.bfloat16)
        acc_ref[j] = jnp.dot(wt, vals, preferred_element_type=jnp.float32)
        m_ref[j] = pm
        t_ref[j] = jnp.sum(wt.astype(jnp.float32), axis=1, keepdims=True)
        return carry

    lax.fori_loop(0, q_ref.shape[0], body, 0)


def attend(slot_query, kv_pool, block=8):
    slots, tok, width = kv_pool.shape
    return pl.pallas_call(
        attn_kernel,
        grid=(slots // block,),
        in_specs=[
            pl.BlockSpec((block, H, HD), lambda i: (i, 0, 0)),
            pl.BlockSpec((block, tok, width), lambda i: (i, 0, 0)),
        ],
        out_specs=[
            pl.BlockSpec((block, H, HD), lambda i: (i, 0, 0)),
            pl.BlockSpec((block, H, 1), lambda i: (i, 0, 0)),
            pl.BlockSpec((block, H, 1), lambda i: (i, 0, 0)),
        ],
        out_shape=[
            jax.ShapeDtypeStruct((slots, H, HD), jnp.float32),
            jax.ShapeDtypeStruct((slots, H, 1), jnp.float32),
            jax.ShapeDtypeStruct((slots, H, 1), jnp.float32),
        ],
    )(slot_query, kv_pool)


def per_device(hidden_in, w_query, w_keyval, w_output, kv_pool, page_table, selected):
    n_page = lax.axis_size("page")
    n_tensor = lax.axis_size("tensor")
    my_page = lax.axis_index("page")
    my_tensor = lax.axis_index("tensor")
    seqs = selected.shape[1]
    groups = H // KVH
    local_heads = H // n_tensor
    scale = 1.0 / math.sqrt(HD)
    slots = kv_pool.shape[0]
    pool_size = page_table.shape[0]
    device = my_page * n_tensor + my_tensor
    position = float(PAGES * PAGE_TOK)
    seq_share = seqs // n_page
    query_cols = w_query.shape[1]
    sub_heads = w_keyval.shape[1] // HD

    my_slots = device * slots + jnp.arange(slots, dtype=jnp.int32)
    match = page_table[None, :] == my_slots[:, None]
    my_logical = jnp.sum(
        jnp.where(match, jnp.arange(pool_size, dtype=jnp.int32)[None, :], 0), axis=1
    )
    seq_of = my_logical // PAGES
    page_of = my_logical % PAGES
    sel_rows = selected[0][seq_of]
    picked = jnp.any(sel_rows == page_of[:, None, None], axis=2)

    tok_all = gather_blocks(hidden_in[0], "tensor", n_tensor).reshape(seqs, -1)
    part_q = jnp.dot(tok_all, w_query, preferred_element_type=jnp.float32)
    part_kv = jnp.dot(tok_all, w_keyval, preferred_element_type=jnp.float32)
    summed = butterfly_sum(jnp.concatenate([part_q, part_kv], axis=1), "page", n_page)
    query = rotate(summed[:, :query_cols].reshape(seqs, local_heads, HD), position)
    query = query.astype(jnp.bfloat16).reshape(seqs, query_cols)
    keyval = summed[:, query_cols:].reshape(seqs, sub_heads, HD)
    kind_ids = (my_tensor * sub_heads + jnp.arange(sub_heads, dtype=jnp.int32)) % 2
    keyval = jnp.where(kind_ids[None, :, None] == 0, rotate(keyval, position), keyval)
    keyval = keyval.reshape(seqs, -1).astype(jnp.bfloat16)
    new_rows = lax.dynamic_slice_in_dim(keyval, my_page * seq_share, seq_share, 0)

    q_all = gather_blocks(query, "tensor", n_tensor)
    q_all = q_all.reshape(KVH, n_tensor // KVH, seqs, local_heads, HD)
    q_all = q_all.transpose(2, 0, 1, 3, 4).reshape(seqs, KVH, groups, HD)
    slot_query = q_all[seq_of]

    page_acc, page_max, page_total = attend(slot_query.reshape(slots, H, HD), kv_pool)
    page_max = page_max.reshape(slots, KVH, groups)
    page_total = page_total.reshape(slots, KVH, groups)
    page_acc = page_acc.reshape(slots, KVH, groups, HD)
    pick = picked[:, :, None]
    page_max = jnp.where(pick, page_max, NEG_BIG).reshape(slots, H)
    page_total = jnp.where(pick, page_total, 0.0).reshape(slots, H)
    page_acc = jnp.where(pick[..., None], page_acc, 0.0).reshape(slots, H, HD)

    owner_rows = jnp.arange(seqs, dtype=jnp.int32)[:, None] == seq_of[None, :]
    owner_hot = owner_rows.astype(jnp.float32)
    loc_max = jnp.max(jnp.where(owner_rows[:, :, None], page_max[None], NEG_BIG), axis=1)
    factor = jnp.exp(page_max - loc_max[seq_of])
    loc_total = jnp.dot(owner_hot, page_total * factor, precision=lax.Precision.HIGHEST)
    loc_acc = jnp.dot(
        owner_hot,
        (page_acc * factor[..., None]).reshape(slots, H * HD),
        precision=lax.Precision.HIGHEST,
    ).reshape(seqs, H, HD)

    packed = jnp.concatenate([loc_acc, loc_total[..., None], loc_max[..., None]], axis=-1)
    width = HD + 2
    packed = packed.reshape(n_page, seq_share, n_tensor, local_heads, width)
    packed = packed.transpose(0, 2, 1, 3, 4).reshape(n_page * n_tensor, -1)
    got = lax.all_to_all(packed, ("page", "tensor"), 0, 0, tiled=True)
    got = got.reshape(n_page * n_tensor, seq_share, local_heads, width)
    src_max = got[..., HD + 1]
    top_max = jnp.max(src_max, axis=0)
    rescale = jnp.exp(src_max - top_max[None])
    full_total = jnp.sum(got[..., HD] * rescale, axis=0)
    full_acc = jnp.sum(got[..., :HD] * rescale[..., None], axis=0)
    heads = (full_acc / full_total[..., None]).astype(jnp.bfloat16)

    heads_all = gather_blocks(heads.reshape(seq_share, local_heads * HD), "page", n_page)
    heads_all = heads_all.reshape(seqs, local_heads * HD)
    part_out = jnp.dot(heads_all, w_output, preferred_element_type=jnp.float32)
    part_out = part_out.reshape(n_tensor, seqs // n_tensor, -1)
    out = jnp.sum(lax.all_to_all(part_out, "tensor", 0, 0, tiled=True), axis=0)
    return (out.astype(jnp.bfloat16)[None], new_rows[None])


def solution(mesh):
    return jax.shard_map(
        per_device,
        mesh=mesh,
        in_specs=(
            P(None, "tensor", "page"),
            P("page", "tensor"),
            P("page", "tensor"),
            P("tensor", "page"),
            P(("page", "tensor"), None, None),
            P(),
            P(),
        ),
        out_specs=(P(None, "tensor", "page"), P(None, "page", "tensor")),
        check_vma=False,
    )
```

```python
import math

import jax
import jax.numpy as jnp
from jax import lax
from jax.experimental import pallas as pl
from jax.experimental.pallas import tpu as pltpu
from jax.sharding import PartitionSpec as P

H = 64
KVH = 8
HD = 128
PAGE_TOK = 64
PAGES = 256


NEG_BIG = -1e30


def frequencies(head_dim):
    half_dim = head_dim // 2
    index = jnp.arange(half_dim, dtype=jnp.float32)
    base_freq = jnp.exp(-(2.0 * index / head_dim) * math.log(500000.0))
    wavelen = 2.0 * math.pi / base_freq
    smooth = (8192.0 / wavelen - 1.0) / 3.0
    middle = (1.0 - smooth) * base_freq / 8.0 + smooth * base_freq
    scaled = jnp.where(wavelen > 8192.0, base_freq / 8.0, base_freq)
    is_middle = jnp.logical_and(wavelen >= 2048.0, wavelen <= 8192.0)
    return jnp.where(is_middle, middle, scaled)


def rotate(vectors, position):
    half_dim = vectors.shape[-1] // 2
    angles = position * frequencies(vectors.shape[-1])
    cosine = jnp.cos(angles)
    sine_v = jnp.sin(angles)
    first_half = vectors[..., :half_dim]
    second_half = vectors[..., half_dim:]
    return jnp.concatenate(
        [first_half * cosine - second_half * sine_v, first_half * sine_v + second_half * cosine],
        axis=-1,
    )


def gather_blocks(x, axis, n):
    return lax.all_to_all(jnp.broadcast_to(x[None], (n,) + x.shape), axis, 0, 0, tiled=True)


def butterfly_sum(x, axis, n):
    d = 1
    while d < n:
        x = x + lax.ppermute(x, axis, [(i, i ^ d) for i in range(n)])
        d *= 2
    return x


def merge_kernel(seq_ref, pick_ref, q_ref, kv_ref, acc_ref, tot_ref, max_ref):
    block = kv_ref.shape[0]
    step = pl.program_id(0)
    scale = 1.0 / math.sqrt(HD)

    @pl.when(step == 0)
    def _init():
        acc_ref[...] = jnp.zeros(acc_ref.shape, jnp.float32)
        tot_ref[...] = jnp.zeros(tot_ref.shape, jnp.float32)
        max_ref[...] = jnp.full(max_ref.shape, NEG_BIG, jnp.float32)

    def body(j, carry):
        slot = step * block + j
        seq = seq_ref[slot]
        for g in range(KVH):
            @pl.when(pick_ref[slot * KVH + g] != 0)
            def _page():
                keys = kv_ref[j, :, pl.ds(g * 2 * HD, HD)]
                vals = kv_ref[j, :, pl.ds(g * 2 * HD + HD, HD)]
                sc = lax.dot_general(q_ref[seq, g], keys, (((1,), (1,)), ((), ())),
                                     preferred_element_type=jnp.float32) * scale
                pm = jnp.max(sc, axis=1, keepdims=True)
                wt = jnp.exp(sc - pm).astype(jnp.bfloat16)
                pt = jnp.sum(wt.astype(jnp.float32), axis=1, keepdims=True)
                pa = jnp.dot(wt, vals, preferred_element_type=jnp.float32)
                m_old = max_ref[seq, g]
                m_new = jnp.maximum(m_old, pm)
                alpha = jnp.exp(m_old - m_new)
                beta = jnp.exp(pm - m_new)
                acc_ref[seq, g] = acc_ref[seq, g] * alpha + pa * beta
                tot_ref[seq, g] = tot_ref[seq, g] * alpha + pt * beta
                max_ref[seq, g] = m_new
        return carry

    lax.fori_loop(0, block, body, 0)

def merge_pages(seq_of, picked, q_all, kv, block=8):
    slots, tok, width = kv.shape
    seqs = q_all.shape[0]
    full = (seqs, KVH, H // KVH, HD)
    grid_spec = pltpu.PrefetchScalarGridSpec(
        num_scalar_prefetch=2,
        grid=(slots // block,),
        in_specs=[pl.BlockSpec(full, lambda i, s, p: (0, 0, 0, 0)),
                  pl.BlockSpec((block, tok, width), lambda i, s, p: (i, 0, 0))],
        out_specs=[pl.BlockSpec(full, lambda i, s, p: (0, 0, 0, 0))] * 3,
    )
    return pl.pallas_call(
        merge_kernel, grid_spec=grid_spec,
        out_shape=[jax.ShapeDtypeStruct(full, jnp.float32)] * 3,
    )(seq_of, picked.reshape(-1).astype(jnp.int32), q_all, kv)


def per_device(hidden_in, w_query, w_keyval, w_output, kv_pool, page_table, selected):
    n_page = lax.axis_size("page")
    n_tensor = lax.axis_size("tensor")
    my_page = lax.axis_index("page")
    my_tensor = lax.axis_index("tensor")
    seqs = selected.shape[1]
    groups = H // KVH
    local_heads = H // n_tensor
    scale = 1.0 / math.sqrt(HD)
    slots = kv_pool.shape[0]
    pool_size = page_table.shape[0]
    device = my_page * n_tensor + my_tensor
    position = float(PAGES * PAGE_TOK)
    seq_share = seqs // n_page
    query_cols = w_query.shape[1]
    sub_heads = w_keyval.shape[1] // HD

    my_slots = device * slots + jnp.arange(slots, dtype=jnp.int32)
    match = page_table[None, :] == my_slots[:, None]
    my_logical = jnp.sum(
        jnp.where(match, jnp.arange(pool_size, dtype=jnp.int32)[None, :], 0), axis=1
    )
    seq_of = my_logical // PAGES
    page_of = my_logical % PAGES
    sel_rows = selected[0][seq_of]
    picked = jnp.any(sel_rows == page_of[:, None, None], axis=2)

    tok_all = gather_blocks(hidden_in[0], "tensor", n_tensor).reshape(seqs, -1)
    part_q = jnp.dot(tok_all, w_query, preferred_element_type=jnp.float32)
    part_kv = jnp.dot(tok_all, w_keyval, preferred_element_type=jnp.float32)
    summed = butterfly_sum(jnp.concatenate([part_q, part_kv], axis=1), "page", n_page)
    query = rotate(summed[:, :query_cols].reshape(seqs, local_heads, HD), position)
    query = query.astype(jnp.bfloat16).reshape(seqs, query_cols)
    keyval = summed[:, query_cols:].reshape(seqs, sub_heads, HD)
    kind_ids = (my_tensor * sub_heads + jnp.arange(sub_heads, dtype=jnp.int32)) % 2
    keyval = jnp.where(kind_ids[None, :, None] == 0, rotate(keyval, position), keyval)
    keyval = keyval.reshape(seqs, -1).astype(jnp.bfloat16)
    new_rows = lax.dynamic_slice_in_dim(keyval, my_page * seq_share, seq_share, 0)

    q_all = gather_blocks(query, "tensor", n_tensor)
    q_all = q_all.reshape(KVH, n_tensor // KVH, seqs, local_heads, HD)
    q_all = q_all.transpose(2, 0, 1, 3, 4).reshape(seqs, KVH, groups, HD)

    loc_acc, loc_total, loc_max = merge_pages(seq_of, picked, q_all, kv_pool)
    loc_acc = loc_acc.reshape(seqs, H, HD)
    loc_total = loc_total[..., 0].reshape(seqs, H)
    loc_max = loc_max[..., 0].reshape(seqs, H)

    packed = jnp.concatenate([loc_acc, loc_total[..., None], loc_max[..., None]], axis=-1)
    width = HD + 2
    packed = packed.reshape(n_page, seq_share, n_tensor, local_heads, width)
    packed = packed.transpose(0, 2, 1, 3, 4).reshape(n_page * n_tensor, -1)
    got = lax.all_to_all(packed, ("page", "tensor"), 0, 0, tiled=True)
    got = got.reshape(n_page * n_tensor, seq_share, local_heads, width)
    src_max = got[..., HD + 1]
    top_max = jnp.max(src_max, axis=0)
    rescale = jnp.exp(src_max - top_max[None])
    full_total = jnp.sum(got[..., HD] * rescale, axis=0)
    full_acc = jnp.sum(got[..., :HD] * rescale[..., None], axis=0)
    heads = (full_acc / full_total[..., None]).astype(jnp.bfloat16)

    heads_all = gather_blocks(heads.reshape(seq_share, local_heads * HD), "page", n_page)
    heads_all = heads_all.reshape(seqs, local_heads * HD)
    part_out = jnp.dot(heads_all, w_output, preferred_element_type=jnp.float32)
    part_out = part_out.reshape(n_tensor, seqs // n_tensor, -1)
    out = jnp.sum(lax.all_to_all(part_out, "tensor", 0, 0, tiled=True), axis=0)
    return (out.astype(jnp.bfloat16)[None], new_rows[None])


def solution(mesh):
    return jax.shard_map(
        per_device,
        mesh=mesh,
        in_specs=(
            P(None, "tensor", "page"),
            P("page", "tensor"),
            P("page", "tensor"),
            P("tensor", "page"),
            P(("page", "tensor"), None, None),
            P(),
            P(),
        ),
        out_specs=(P(None, "tensor", "page"), P(None, "page", "tensor")),
        check_vma=False,
    )
```

```python
import math

import jax
import jax.numpy as jnp
from jax import lax
from jax.experimental import pallas as pl
from jax.experimental.pallas import tpu as pltpu
from jax.sharding import PartitionSpec as P

H = 64
KVH = 8
HD = 128
PAGE_TOK = 64
PAGES = 256


NEG_BIG = -1e30


def frequencies(head_dim):
    half_dim = head_dim // 2
    index = jnp.arange(half_dim, dtype=jnp.float32)
    base_freq = jnp.exp(-(2.0 * index / head_dim) * math.log(500000.0))
    wavelen = 2.0 * math.pi / base_freq
    smooth = (8192.0 / wavelen - 1.0) / 3.0
    middle = (1.0 - smooth) * base_freq / 8.0 + smooth * base_freq
    scaled = jnp.where(wavelen > 8192.0, base_freq / 8.0, base_freq)
    is_middle = jnp.logical_and(wavelen >= 2048.0, wavelen <= 8192.0)
    return jnp.where(is_middle, middle, scaled)


def rotate(vectors, position):
    half_dim = vectors.shape[-1] // 2
    angles = position * frequencies(vectors.shape[-1])
    cosine = jnp.cos(angles)
    sine_v = jnp.sin(angles)
    first_half = vectors[..., :half_dim]
    second_half = vectors[..., half_dim:]
    return jnp.concatenate(
        [first_half * cosine - second_half * sine_v, first_half * sine_v + second_half * cosine],
        axis=-1,
    )


def gather_blocks(x, axis, n):
    return lax.all_to_all(jnp.broadcast_to(x[None], (n,) + x.shape), axis, 0, 0, tiled=True)


def butterfly_sum(x, axis, n):
    d = 1
    while d < n:
        x = x + lax.ppermute(x, axis, [(i, i ^ d) for i in range(n)])
        d *= 2
    return x


DEPTH = 8

def merge_kernel(seq_ref, pick_ref, q_ref, kv_hbm, acc_ref, tot_ref, max_ref, order_ref, buf, sems):
    pairs = pick_ref.shape[0]
    scale = 1.0 / math.sqrt(HD)
    acc_ref[...] = jnp.zeros(acc_ref.shape, jnp.float32)
    tot_ref[...] = jnp.zeros(tot_ref.shape, jnp.float32)
    max_ref[...] = jnp.full(max_ref.shape, NEG_BIG, jnp.float32)

    def compact(i, n):
        order_ref[n] = i
        return n + pick_ref[i]

    count = lax.fori_loop(0, pairs, compact, 0)

    def copy_of(k):
        e = order_ref[k]
        slot = e // KVH
        g = e % KVH
        return pltpu.make_async_copy(
            kv_hbm.at[slot, :, pl.ds(g * 2 * HD, 2 * HD)], buf.at[k % DEPTH], sems.at[k % DEPTH]
        )

    for k in range(DEPTH):
        @pl.when(k < count)
        def _start():
            copy_of(k).start()

    def body(k, carry):
        e = order_ref[k]
        slot = e // KVH
        g = e % KVH
        seq = seq_ref[slot]
        copy_of(k).wait()
        page = buf[k % DEPTH]
        keys = page[:, :HD]
        vals = page[:, HD:]
        sc = lax.dot_general(q_ref[seq, g], keys, (((1,), (1,)), ((), ())),
                             preferred_element_type=jnp.float32) * scale
        pm = jnp.max(sc, axis=1, keepdims=True)
        wt = jnp.exp(sc - pm).astype(jnp.bfloat16)
        pt = jnp.sum(wt.astype(jnp.float32), axis=1, keepdims=True)
        pa = jnp.dot(wt, vals, preferred_element_type=jnp.float32)

        @pl.when(k + DEPTH < count)
        def _next():
            copy_of(k + DEPTH).start()

        m_old = max_ref[seq, g]
        m_new = jnp.maximum(m_old, pm)
        alpha = jnp.exp(m_old - m_new)
        beta = jnp.exp(pm - m_new)
        acc_ref[seq, g] = acc_ref[seq, g] * alpha + pa * beta
        tot_ref[seq, g] = tot_ref[seq, g] * alpha + pt * beta
        max_ref[seq, g] = m_new
        return carry

    lax.fori_loop(0, count, body, 0)


def merge_pages(seq_of, picked, q_all, kv):
    slots, tok, width = kv.shape
    seqs = q_all.shape[0]
    full = (seqs, KVH, H // KVH, HD)
    vmem = pl.BlockSpec(memory_space=pltpu.VMEM)
    smem = pl.BlockSpec(memory_space=pltpu.SMEM)
    return pl.pallas_call(
        merge_kernel,
        in_specs=[smem, smem, vmem, pl.BlockSpec(memory_space=pl.ANY)],
        out_specs=[vmem] * 3,
        out_shape=[jax.ShapeDtypeStruct(full, jnp.float32)] * 3,
        scratch_shapes=[
            pltpu.SMEM((slots * KVH,), jnp.int32),
            pltpu.VMEM((DEPTH, tok, 2 * HD), kv.dtype),
            pltpu.SemaphoreType.DMA((DEPTH,)),
        ],
    )(seq_of, picked.reshape(-1).astype(jnp.int32), q_all, kv)


def per_device(hidden_in, w_query, w_keyval, w_output, kv_pool, page_table, selected):
    n_page = lax.axis_size("page")
    n_tensor = lax.axis_size("tensor")
    my_page = lax.axis_index("page")
    my_tensor = lax.axis_index("tensor")
    seqs = selected.shape[1]
    groups = H // KVH
    local_heads = H // n_tensor
    scale = 1.0 / math.sqrt(HD)
    slots = kv_pool.shape[0]
    pool_size = page_table.shape[0]
    device = my_page * n_tensor + my_tensor
    position = float(PAGES * PAGE_TOK)
    seq_share = seqs // n_page
    query_cols = w_query.shape[1]
    sub_heads = w_keyval.shape[1] // HD

    my_slots = device * slots + jnp.arange(slots, dtype=jnp.int32)
    match = page_table[None, :] == my_slots[:, None]
    my_logical = jnp.sum(
        jnp.where(match, jnp.arange(pool_size, dtype=jnp.int32)[None, :], 0), axis=1
    )
    seq_of = my_logical // PAGES
    page_of = my_logical % PAGES
    sel_rows = selected[0][seq_of]
    picked = jnp.any(sel_rows == page_of[:, None, None], axis=2)

    tok_all = gather_blocks(hidden_in[0], "tensor", n_tensor).reshape(seqs, -1)
    part_q = jnp.dot(tok_all, w_query, preferred_element_type=jnp.float32)
    part_kv = jnp.dot(tok_all, w_keyval, preferred_element_type=jnp.float32)
    summed = butterfly_sum(jnp.concatenate([part_q, part_kv], axis=1), "page", n_page)
    query = rotate(summed[:, :query_cols].reshape(seqs, local_heads, HD), position)
    query = query.astype(jnp.bfloat16).reshape(seqs, query_cols)
    keyval = summed[:, query_cols:].reshape(seqs, sub_heads, HD)
    kind_ids = (my_tensor * sub_heads + jnp.arange(sub_heads, dtype=jnp.int32)) % 2
    keyval = jnp.where(kind_ids[None, :, None] == 0, rotate(keyval, position), keyval)
    keyval = keyval.reshape(seqs, -1).astype(jnp.bfloat16)
    new_rows = lax.dynamic_slice_in_dim(keyval, my_page * seq_share, seq_share, 0)

    q_all = gather_blocks(query, "tensor", n_tensor)
    q_all = q_all.reshape(KVH, n_tensor // KVH, seqs, local_heads, HD)
    q_all = q_all.transpose(2, 0, 1, 3, 4).reshape(seqs, KVH, groups, HD)

    loc_acc, loc_total, loc_max = merge_pages(seq_of, picked, q_all, kv_pool)
    loc_acc = loc_acc.reshape(seqs, H, HD)
    loc_total = loc_total[..., 0].reshape(seqs, H)
    loc_max = loc_max[..., 0].reshape(seqs, H)

    packed = jnp.concatenate([loc_acc, loc_total[..., None], loc_max[..., None]], axis=-1)
    width = HD + 2
    packed = packed.reshape(n_page, seq_share, n_tensor, local_heads, width)
    packed = packed.transpose(0, 2, 1, 3, 4).reshape(n_page * n_tensor, -1)
    got = lax.all_to_all(packed, ("page", "tensor"), 0, 0, tiled=True)
    got = got.reshape(n_page * n_tensor, seq_share, local_heads, width)
    src_max = got[..., HD + 1]
    top_max = jnp.max(src_max, axis=0)
    rescale = jnp.exp(src_max - top_max[None])
    full_total = jnp.sum(got[..., HD] * rescale, axis=0)
    full_acc = jnp.sum(got[..., :HD] * rescale[..., None], axis=0)
    heads = (full_acc / full_total[..., None]).astype(jnp.bfloat16)

    heads_all = gather_blocks(heads.reshape(seq_share, local_heads * HD), "page", n_page)
    heads_all = heads_all.reshape(seqs, local_heads * HD)
    part_out = jnp.dot(heads_all, w_output, preferred_element_type=jnp.float32)
    part_out = part_out.reshape(n_tensor, seqs // n_tensor, -1)
    out = jnp.sum(lax.all_to_all(part_out, "tensor", 0, 0, tiled=True), axis=0)
    return (out.astype(jnp.bfloat16)[None], new_rows[None])


def solution(mesh):
    return jax.shard_map(
        per_device,
        mesh=mesh,
        in_specs=(
            P(None, "tensor", "page"),
            P("page", "tensor"),
            P("page", "tensor"),
            P("tensor", "page"),
            P(("page", "tensor"), None, None),
            P(),
            P(),
        ),
        out_specs=(P(None, "tensor", "page"), P(None, "page", "tensor")),
        check_vma=False,
    )
```

```python
import math

import jax
import jax.numpy as jnp
from jax import lax
from jax.experimental import pallas as pl
from jax.experimental.pallas import tpu as pltpu
from jax.sharding import PartitionSpec as P

H = 64
KVH = 8
HD = 128
PAGE_TOK = 64
PAGES = 256


NEG_BIG = -1e30


def frequencies(head_dim):
    half_dim = head_dim // 2
    index = jnp.arange(half_dim, dtype=jnp.float32)
    base_freq = jnp.exp(-(2.0 * index / head_dim) * math.log(500000.0))
    wavelen = 2.0 * math.pi / base_freq
    smooth = (8192.0 / wavelen - 1.0) / 3.0
    middle = (1.0 - smooth) * base_freq / 8.0 + smooth * base_freq
    scaled = jnp.where(wavelen > 8192.0, base_freq / 8.0, base_freq)
    is_middle = jnp.logical_and(wavelen >= 2048.0, wavelen <= 8192.0)
    return jnp.where(is_middle, middle, scaled)


def rotate(vectors, position):
    half_dim = vectors.shape[-1] // 2
    angles = position * frequencies(vectors.shape[-1])
    cosine = jnp.cos(angles)
    sine_v = jnp.sin(angles)
    first_half = vectors[..., :half_dim]
    second_half = vectors[..., half_dim:]
    return jnp.concatenate(
        [first_half * cosine - second_half * sine_v, first_half * sine_v + second_half * cosine],
        axis=-1,
    )


def gather_blocks(x, axis, n):
    return lax.all_to_all(jnp.broadcast_to(x[None], (n,) + x.shape), axis, 0, 0, tiled=True)


def butterfly_sum(x, axis, n):
    d = 1
    while d < n:
        x = x + lax.ppermute(x, axis, [(i, i ^ d) for i in range(n)])
        d *= 2
    return x


DEPTH = 8
UNROLL = 4

def merge_kernel(seq_ref, pick_ref, q_ref, kv_hbm, acc_ref, tot_ref, max_ref, order_ref, buf, sems):
    pairs = pick_ref.shape[0]
    scale = 1.0 / math.sqrt(HD)
    acc_ref[...] = jnp.zeros(acc_ref.shape, jnp.float32)
    tot_ref[...] = jnp.zeros(tot_ref.shape, jnp.float32)
    max_ref[...] = jnp.full(max_ref.shape, NEG_BIG, jnp.float32)

    def compact(i, n):
        order_ref[n] = i
        return n + pick_ref[i]

    count = lax.fori_loop(0, pairs, compact, 0)
    padded = (count + UNROLL - 1) // UNROLL * UNROLL

    def pad(k, carry):
        order_ref[k] = 0
        return carry

    lax.fori_loop(count, padded, pad, 0)

    def copy_of(k):
        e = order_ref[k]
        slot = e // KVH
        g = e % KVH
        return pltpu.make_async_copy(
            kv_hbm.at[slot, :, pl.ds(g * 2 * HD, 2 * HD)], buf.at[k % DEPTH], sems.at[k % DEPTH]
        )

    for k in range(DEPTH):
        @pl.when(k < padded)
        def _start():
            copy_of(k).start()

    def attend(k):
        e = order_ref[k]
        g = e % KVH
        seq = seq_ref[e // KVH]
        copy_of(k).wait()
        page = buf[k % DEPTH]
        sc = lax.dot_general(q_ref[seq, g], page[:, :HD], (((1,), (1,)), ((), ())),
                             preferred_element_type=jnp.float32) * scale
        pm = jnp.max(sc, axis=1, keepdims=True)
        wt = jnp.exp(sc - pm).astype(jnp.bfloat16)
        pt = jnp.sum(wt.astype(jnp.float32), axis=1, keepdims=True)
        pa = jnp.dot(wt, page[:, HD:], preferred_element_type=jnp.float32)
        return seq, g, pm, pt, pa

    def update(seq, g, pm, pt, pa, live):
        m_old = max_ref[seq, g]
        m_new = jnp.where(live, jnp.maximum(m_old, pm), m_old)
        alpha = jnp.exp(m_old - m_new)
        beta = jnp.where(live, jnp.exp(pm - m_new), 0.0)
        acc_ref[seq, g] = acc_ref[seq, g] * alpha + pa * beta
        tot_ref[seq, g] = tot_ref[seq, g] * alpha + pt * beta
        max_ref[seq, g] = m_new

    def body(step, carry):
        ks = [step * UNROLL + u for u in range(UNROLL)]
        done = [attend(k) for k in ks]
        for k in ks:
            @pl.when(k + DEPTH < padded)
            def _next():
                copy_of(k + DEPTH).start()
        for k, res in zip(ks, done):
            update(*res, k < count)
        return carry

    lax.fori_loop(0, padded // UNROLL, body, 0)


def merge_pages(seq_of, picked, q_all, kv):
    slots, tok, width = kv.shape
    seqs = q_all.shape[0]
    full = (seqs, KVH, H // KVH, HD)
    vmem = pl.BlockSpec(memory_space=pltpu.VMEM)
    smem = pl.BlockSpec(memory_space=pltpu.SMEM)
    return pl.pallas_call(
        merge_kernel,
        in_specs=[smem, smem, vmem, pl.BlockSpec(memory_space=pl.ANY)],
        out_specs=[vmem] * 3,
        out_shape=[jax.ShapeDtypeStruct(full, jnp.float32)] * 3,
        scratch_shapes=[
            pltpu.SMEM((slots * KVH,), jnp.int32),
            pltpu.VMEM((DEPTH, tok, 2 * HD), kv.dtype),
            pltpu.SemaphoreType.DMA((DEPTH,)),
        ],
    )(seq_of, picked.reshape(-1).astype(jnp.int32), q_all, kv)


def per_device(hidden_in, w_query, w_keyval, w_output, kv_pool, page_table, selected):
    n_page = lax.axis_size("page")
    n_tensor = lax.axis_size("tensor")
    my_page = lax.axis_index("page")
    my_tensor = lax.axis_index("tensor")
    seqs = selected.shape[1]
    groups = H // KVH
    local_heads = H // n_tensor
    scale = 1.0 / math.sqrt(HD)
    slots = kv_pool.shape[0]
    pool_size = page_table.shape[0]
    device = my_page * n_tensor + my_tensor
    position = float(PAGES * PAGE_TOK)
    seq_share = seqs // n_page
    query_cols = w_query.shape[1]
    sub_heads = w_keyval.shape[1] // HD

    my_slots = device * slots + jnp.arange(slots, dtype=jnp.int32)
    match = page_table[None, :] == my_slots[:, None]
    my_logical = jnp.sum(
        jnp.where(match, jnp.arange(pool_size, dtype=jnp.int32)[None, :], 0), axis=1
    )
    seq_of = my_logical // PAGES
    page_of = my_logical % PAGES
    sel_rows = selected[0][seq_of]
    picked = jnp.any(sel_rows == page_of[:, None, None], axis=2)

    tok_all = gather_blocks(hidden_in[0], "tensor", n_tensor).reshape(seqs, -1)
    part_q = jnp.dot(tok_all, w_query, preferred_element_type=jnp.float32)
    part_kv = jnp.dot(tok_all, w_keyval, preferred_element_type=jnp.float32)
    summed = butterfly_sum(jnp.concatenate([part_q, part_kv], axis=1), "page", n_page)
    query = rotate(summed[:, :query_cols].reshape(seqs, local_heads, HD), position)
    query = query.astype(jnp.bfloat16).reshape(seqs, query_cols)
    keyval = summed[:, query_cols:].reshape(seqs, sub_heads, HD)
    kind_ids = (my_tensor * sub_heads + jnp.arange(sub_heads, dtype=jnp.int32)) % 2
    keyval = jnp.where(kind_ids[None, :, None] == 0, rotate(keyval, position), keyval)
    keyval = keyval.reshape(seqs, -1).astype(jnp.bfloat16)
    new_rows = lax.dynamic_slice_in_dim(keyval, my_page * seq_share, seq_share, 0)

    q_all = gather_blocks(query, "tensor", n_tensor)
    q_all = q_all.reshape(KVH, n_tensor // KVH, seqs, local_heads, HD)
    q_all = q_all.transpose(2, 0, 1, 3, 4).reshape(seqs, KVH, groups, HD)

    loc_acc, loc_total, loc_max = merge_pages(seq_of, picked, q_all, kv_pool)
    loc_acc = loc_acc.reshape(seqs, H, HD)
    loc_total = loc_total[..., 0].reshape(seqs, H)
    loc_max = loc_max[..., 0].reshape(seqs, H)

    packed = jnp.concatenate([loc_acc, loc_total[..., None], loc_max[..., None]], axis=-1)
    width = HD + 2
    packed = packed.reshape(n_page, seq_share, n_tensor, local_heads, width)
    packed = packed.transpose(0, 2, 1, 3, 4).reshape(n_page * n_tensor, -1)
    got = lax.all_to_all(packed, ("page", "tensor"), 0, 0, tiled=True)
    got = got.reshape(n_page * n_tensor, seq_share, local_heads, width)
    src_max = got[..., HD + 1]
    top_max = jnp.max(src_max, axis=0)
    rescale = jnp.exp(src_max - top_max[None])
    full_total = jnp.sum(got[..., HD] * rescale, axis=0)
    full_acc = jnp.sum(got[..., :HD] * rescale[..., None], axis=0)
    heads = (full_acc / full_total[..., None]).astype(jnp.bfloat16)

    heads_all = gather_blocks(heads.reshape(seq_share, local_heads * HD), "page", n_page)
    heads_all = heads_all.reshape(seqs, local_heads * HD)
    part_out = jnp.dot(heads_all, w_output, preferred_element_type=jnp.float32)
    part_out = part_out.reshape(n_tensor, seqs // n_tensor, -1)
    out = jnp.sum(lax.all_to_all(part_out, "tensor", 0, 0, tiled=True), axis=0)
    return (out.astype(jnp.bfloat16)[None], new_rows[None])


def solution(mesh):
    return jax.shard_map(
        per_device,
        mesh=mesh,
        in_specs=(
            P(None, "tensor", "page"),
            P("page", "tensor"),
            P("page", "tensor"),
            P("tensor", "page"),
            P(("page", "tensor"), None, None),
            P(),
            P(),
        ),
        out_specs=(P(None, "tensor", "page"), P(None, "page", "tensor")),
        check_vma=False,
    )
```

```python
import math

import jax
import jax.numpy as jnp
from jax import lax
from jax.experimental import pallas as pl
from jax.experimental.pallas import tpu as pltpu
from jax.sharding import PartitionSpec as P

H = 64
KVH = 8
HD = 128
PAGE_TOK = 64
PAGES = 256


NEG_BIG = -1e30


def frequencies(head_dim):
    half_dim = head_dim // 2
    index = jnp.arange(half_dim, dtype=jnp.float32)
    base_freq = jnp.exp(-(2.0 * index / head_dim) * math.log(500000.0))
    wavelen = 2.0 * math.pi / base_freq
    smooth = (8192.0 / wavelen - 1.0) / 3.0
    middle = (1.0 - smooth) * base_freq / 8.0 + smooth * base_freq
    scaled = jnp.where(wavelen > 8192.0, base_freq / 8.0, base_freq)
    is_middle = jnp.logical_and(wavelen >= 2048.0, wavelen <= 8192.0)
    return jnp.where(is_middle, middle, scaled)


def rotate(vectors, position):
    half_dim = vectors.shape[-1] // 2
    angles = position * frequencies(vectors.shape[-1])
    cosine = jnp.cos(angles)
    sine_v = jnp.sin(angles)
    first_half = vectors[..., :half_dim]
    second_half = vectors[..., half_dim:]
    return jnp.concatenate(
        [first_half * cosine - second_half * sine_v, first_half * sine_v + second_half * cosine],
        axis=-1,
    )


def gather_blocks(x, axis, n):
    return lax.all_to_all(jnp.broadcast_to(x[None], (n,) + x.shape), axis, 0, 0, tiled=True)


def butterfly_sum(x, axis, n):
    d = 1
    while d < n:
        x = x + lax.ppermute(x, axis, [(i, i ^ d) for i in range(n)])
        d *= 2
    return x


DEPTH = 8
UNROLL = 4

def merge_kernel(seq_ref, order_ref, count_ref, q_ref, kv_hbm, acc_ref, tot_ref, max_ref, buf, sems):
    scale = 1.0 / math.sqrt(HD)
    acc_ref[...] = jnp.zeros(acc_ref.shape, jnp.float32)
    tot_ref[...] = jnp.zeros(tot_ref.shape, jnp.float32)
    max_ref[...] = jnp.full(max_ref.shape, NEG_BIG, jnp.float32)

    count = count_ref[0]
    padded = (count + UNROLL - 1) // UNROLL * UNROLL

    def copy_of(k):
        e = order_ref[k]
        slot = e // KVH
        g = e % KVH
        return pltpu.make_async_copy(
            kv_hbm.at[slot, :, pl.ds(g * 2 * HD, 2 * HD)], buf.at[k % DEPTH], sems.at[k % DEPTH]
        )

    for k in range(DEPTH):
        @pl.when(k < padded)
        def _start():
            copy_of(k).start()

    def attend(k):
        e = order_ref[k]
        g = e % KVH
        seq = seq_ref[e // KVH]
        page = buf[k % DEPTH]
        sc = lax.dot_general(q_ref[seq, g], page[:, :HD], (((1,), (1,)), ((), ())),
                             preferred_element_type=jnp.float32) * scale
        pm = jnp.max(sc, axis=1, keepdims=True)
        wt = jnp.exp(sc - pm).astype(jnp.bfloat16)
        pt = jnp.sum(wt.astype(jnp.float32), axis=1, keepdims=True)
        pa = jnp.dot(wt, page[:, HD:], preferred_element_type=jnp.float32)
        return seq, g, pm, pt, pa

    def update(seq, g, pm, pt, pa, live):
        m_old = max_ref[seq, g]
        m_new = jnp.where(live, jnp.maximum(m_old, pm), m_old)
        alpha = jnp.exp(m_old - m_new)
        beta = jnp.where(live, jnp.exp(pm - m_new), 0.0)
        acc_ref[seq, g] = acc_ref[seq, g] * alpha + pa * beta
        tot_ref[seq, g] = tot_ref[seq, g] * alpha + pt * beta
        max_ref[seq, g] = m_new

    def body(step, carry):
        ks = [step * UNROLL + u for u in range(UNROLL)]
        for k in ks:
            copy_of(k).wait()
        done = [attend(k) for k in ks]
        for k, res in zip(ks, done):
            update(*res, k < count)
        for k in ks:
            @pl.when(k + DEPTH < padded)
            def _next():
                copy_of(k + DEPTH).start()
        return carry

    lax.fori_loop(0, padded // UNROLL, body, 0)


def merge_pages(seq_of, picked, q_all, kv):
    slots, tok, width = kv.shape
    seqs = q_all.shape[0]
    full = (seqs, KVH, H // KVH, HD)
    flags = picked.reshape(-1).astype(jnp.int32)
    pairs = flags.shape[0]
    place = jnp.cumsum(flags) - 1
    hit = (place[None, :] == jnp.arange(pairs, dtype=jnp.int32)[:, None]) & (flags[None, :] == 1)
    order = jnp.sum(jnp.where(hit, jnp.arange(pairs, dtype=jnp.int32)[None, :], 0), axis=1)
    count = jnp.sum(flags, keepdims=True)
    vmem = pl.BlockSpec(memory_space=pltpu.VMEM)
    smem = pl.BlockSpec(memory_space=pltpu.SMEM)
    return pl.pallas_call(
        merge_kernel,
        in_specs=[smem, smem, smem, vmem, pl.BlockSpec(memory_space=pl.ANY)],
        out_specs=[vmem] * 3,
        out_shape=[jax.ShapeDtypeStruct(full, jnp.float32)] * 3,
        scratch_shapes=[
            pltpu.VMEM((DEPTH, tok, 2 * HD), kv.dtype),
            pltpu.SemaphoreType.DMA((DEPTH,)),
        ],
    )(seq_of, order, count, q_all, kv)


def per_device(hidden_in, w_query, w_keyval, w_output, kv_pool, page_table, selected):
    n_page = lax.axis_size("page")
    n_tensor = lax.axis_size("tensor")
    my_page = lax.axis_index("page")
    my_tensor = lax.axis_index("tensor")
    seqs = selected.shape[1]
    groups = H // KVH
    local_heads = H // n_tensor
    scale = 1.0 / math.sqrt(HD)
    slots = kv_pool.shape[0]
    pool_size = page_table.shape[0]
    device = my_page * n_tensor + my_tensor
    position = float(PAGES * PAGE_TOK)
    seq_share = seqs // n_page
    query_cols = w_query.shape[1]
    sub_heads = w_keyval.shape[1] // HD

    my_slots = device * slots + jnp.arange(slots, dtype=jnp.int32)
    match = page_table[None, :] == my_slots[:, None]
    my_logical = jnp.sum(
        jnp.where(match, jnp.arange(pool_size, dtype=jnp.int32)[None, :], 0), axis=1
    )
    seq_of = my_logical // PAGES
    page_of = my_logical % PAGES
    sel_rows = selected[0][seq_of]
    picked = jnp.any(sel_rows == page_of[:, None, None], axis=2)

    tok_all = gather_blocks(hidden_in[0], "tensor", n_tensor).reshape(seqs, -1)
    part_q = jnp.dot(tok_all, w_query, preferred_element_type=jnp.float32)
    part_kv = jnp.dot(tok_all, w_keyval, preferred_element_type=jnp.float32)
    summed = butterfly_sum(jnp.concatenate([part_q, part_kv], axis=1), "page", n_page)
    query = rotate(summed[:, :query_cols].reshape(seqs, local_heads, HD), position)
    query = query.astype(jnp.bfloat16).reshape(seqs, query_cols)
    keyval = summed[:, query_cols:].reshape(seqs, sub_heads, HD)
    kind_ids = (my_tensor * sub_heads + jnp.arange(sub_heads, dtype=jnp.int32)) % 2
    keyval = jnp.where(kind_ids[None, :, None] == 0, rotate(keyval, position), keyval)
    keyval = keyval.reshape(seqs, -1).astype(jnp.bfloat16)
    new_rows = lax.dynamic_slice_in_dim(keyval, my_page * seq_share, seq_share, 0)

    q_all = gather_blocks(query, "tensor", n_tensor)
    q_all = q_all.reshape(KVH, n_tensor // KVH, seqs, local_heads, HD)
    q_all = q_all.transpose(2, 0, 1, 3, 4).reshape(seqs, KVH, groups, HD)

    loc_acc, loc_total, loc_max = merge_pages(seq_of, picked, q_all, kv_pool)
    loc_acc = loc_acc.reshape(seqs, H, HD)
    loc_total = loc_total[..., 0].reshape(seqs, H)
    loc_max = loc_max[..., 0].reshape(seqs, H)

    blocks = n_page * n_tensor
    def by_owner(x):
        x = x.reshape((n_page, seq_share, n_tensor, local_heads) + x.shape[2:])
        return x.transpose((0, 2, 1, 3) + tuple(range(4, x.ndim))).reshape(blocks, -1)
    rows = seq_share * local_heads
    packed = jnp.concatenate([by_owner(loc_acc), by_owner(loc_total), by_owner(loc_max)], axis=1)
    got = lax.all_to_all(packed, ("page", "tensor"), 0, 0, tiled=True)
    src_acc = got[:, :rows * HD].reshape(blocks, rows, HD)
    src_total = got[:, rows * HD:rows * HD + rows]
    src_max = got[:, rows * HD + rows:]
    top_max = jnp.max(src_max, axis=0)
    rescale = jnp.exp(src_max - top_max[None])
    full_total = jnp.sum(src_total * rescale, axis=0)
    full_acc = jnp.sum(src_acc * rescale[..., None], axis=0)
    heads = (full_acc / full_total[..., None]).astype(jnp.bfloat16)

    heads_all = gather_blocks(heads.reshape(seq_share, local_heads * HD), "page", n_page)
    heads_all = heads_all.reshape(seqs, local_heads * HD)
    part_out = jnp.dot(heads_all, w_output, preferred_element_type=jnp.float32)
    part_out = part_out.reshape(n_tensor, seqs // n_tensor, -1)
    out = jnp.sum(lax.all_to_all(part_out, "tensor", 0, 0, tiled=True), axis=0)
    return (out.astype(jnp.bfloat16)[None], new_rows[None])


def solution(mesh):
    return jax.shard_map(
        per_device,
        mesh=mesh,
        in_specs=(
            P(None, "tensor", "page"),
            P("page", "tensor"),
            P("page", "tensor"),
            P("tensor", "page"),
            P(("page", "tensor"), None, None),
            P(),
            P(),
        ),
        out_specs=(P(None, "tensor", "page"), P(None, "page", "tensor")),
        check_vma=False,
    )
```

```python
import math

import jax
import jax.numpy as jnp
from jax import lax
from jax.experimental import pallas as pl
from jax.experimental.pallas import tpu as pltpu
from jax.sharding import PartitionSpec as P

H = 64
KVH = 8
HD = 128
PAGE_TOK = 64
PAGES = 256


NEG_BIG = -1e30


def frequencies(head_dim):
    half_dim = head_dim // 2
    index = jnp.arange(half_dim, dtype=jnp.float32)
    base_freq = jnp.exp(-(2.0 * index / head_dim) * math.log(500000.0))
    wavelen = 2.0 * math.pi / base_freq
    smooth = (8192.0 / wavelen - 1.0) / 3.0
    middle = (1.0 - smooth) * base_freq / 8.0 + smooth * base_freq
    scaled = jnp.where(wavelen > 8192.0, base_freq / 8.0, base_freq)
    is_middle = jnp.logical_and(wavelen >= 2048.0, wavelen <= 8192.0)
    return jnp.where(is_middle, middle, scaled)


def rotate(vectors, position):
    half_dim = vectors.shape[-1] // 2
    angles = position * frequencies(vectors.shape[-1])
    cosine = jnp.cos(angles)
    sine_v = jnp.sin(angles)
    first_half = vectors[..., :half_dim]
    second_half = vectors[..., half_dim:]
    return jnp.concatenate(
        [first_half * cosine - second_half * sine_v, first_half * sine_v + second_half * cosine],
        axis=-1,
    )


def gather_blocks(x, axis, n):
    return lax.all_to_all(jnp.broadcast_to(x[None], (n,) + x.shape), axis, 0, 0, tiled=True)


def butterfly_sum(x, axis, n):
    d = 1
    while d < n:
        x = x + lax.ppermute(x, axis, [(i, i ^ d) for i in range(n)])
        d *= 2
    return x


DEPTH = 32
UNROLL = 16

def merge_kernel(seq_ref, order_ref, count_ref, q_ref, kv_hbm, acc_ref, tot_ref, max_ref, buf, sems):
    scale = 1.0 / math.sqrt(HD)
    acc_ref[...] = jnp.zeros(acc_ref.shape, jnp.float32)
    tot_ref[...] = jnp.zeros(tot_ref.shape, jnp.float32)
    max_ref[...] = jnp.full(max_ref.shape, NEG_BIG, jnp.float32)

    count = count_ref[0]
    padded = (count + UNROLL - 1) // UNROLL * UNROLL

    def copy_of(k):
        e = order_ref[k]
        slot = e // KVH
        g = e % KVH
        return pltpu.make_async_copy(
            kv_hbm.at[slot, :, pl.ds(g * 2 * HD, 2 * HD)], buf.at[k % DEPTH], sems.at[k % DEPTH]
        )

    for k in range(DEPTH):
        @pl.when(k < padded)
        def _start():
            copy_of(k).start()

    rows = lax.broadcasted_iota(jnp.int32, (UNROLL * 8, UNROLL * 64), 0) // 8
    cols = lax.broadcasted_iota(jnp.int32, (UNROLL * 8, UNROLL * 64), 1) // 64
    own_page = rows == cols

    def attend_all(ks):
        where = []
        qs, keys, vals = [], [], []
        for k in ks:
            e = order_ref[k]
            g = e % KVH
            seq = seq_ref[e // KVH]
            page = buf[k % DEPTH]
            where.append((seq, g))
            qs.append(q_ref[seq, g])
            keys.append(page[:, :HD])
            vals.append(page[:, HD:])
        sc = lax.dot_general(jnp.concatenate(qs, axis=0), jnp.concatenate(keys, axis=0),
                             (((1,), (1,)), ((), ())), preferred_element_type=jnp.float32) * scale
        sc = jnp.where(own_page, sc, -jnp.inf)
        pm = jnp.max(sc, axis=1, keepdims=True)
        wt = jnp.exp(sc - pm).astype(jnp.bfloat16)
        pt = jnp.sum(wt.astype(jnp.float32), axis=1, keepdims=True)
        pa = jnp.dot(wt, jnp.concatenate(vals, axis=0), preferred_element_type=jnp.float32)
        rows8 = [slice(8 * u, 8 * u + 8) for u in range(len(ks))]
        return [(seq, g, pm[r], pt[r], pa[r]) for (seq, g), r in zip(where, rows8)]

    def update(seq, g, pm, pt, pa, live):
        m_old = max_ref[seq, g]
        m_new = jnp.where(live, jnp.maximum(m_old, pm), m_old)
        alpha = jnp.exp(m_old - m_new)
        beta = jnp.where(live, jnp.exp(pm - m_new), 0.0)
        acc_ref[seq, g] = acc_ref[seq, g] * alpha + pa * beta
        tot_ref[seq, g] = tot_ref[seq, g] * alpha + pt * beta
        max_ref[seq, g] = m_new

    def body(step, carry):
        ks = [step * UNROLL + u for u in range(UNROLL)]
        for k in ks:
            copy_of(k).wait()
        done = attend_all(ks)
        for k, res in zip(ks, done):
            update(*res, k < count)
        for k in ks:
            @pl.when(k + DEPTH < padded)
            def _next():
                copy_of(k + DEPTH).start()
        return carry

    lax.fori_loop(0, padded // UNROLL, body, 0)


def merge_pages(seq_of, picked, q_all, kv):
    slots, tok, width = kv.shape
    seqs = q_all.shape[0]
    full = (seqs, KVH, H // KVH, HD)
    flags = picked.reshape(-1).astype(jnp.int32)
    pairs = flags.shape[0]
    place = jnp.cumsum(flags) - 1
    hit = (place[None, :] == jnp.arange(pairs, dtype=jnp.int32)[:, None]) & (flags[None, :] == 1)
    order = jnp.sum(jnp.where(hit, jnp.arange(pairs, dtype=jnp.int32)[None, :], 0), axis=1)
    count = jnp.sum(flags, keepdims=True)
    vmem = pl.BlockSpec(memory_space=pltpu.VMEM)
    smem = pl.BlockSpec(memory_space=pltpu.SMEM)
    return pl.pallas_call(
        merge_kernel,
        in_specs=[smem, smem, smem, vmem, pl.BlockSpec(memory_space=pl.ANY)],
        out_specs=[vmem] * 3,
        out_shape=[jax.ShapeDtypeStruct(full, jnp.float32)] * 3,
        scratch_shapes=[
            pltpu.VMEM((DEPTH, tok, 2 * HD), kv.dtype),
            pltpu.SemaphoreType.DMA((DEPTH,)),
        ],
    )(seq_of, order, count, q_all, kv)


def per_device(hidden_in, w_query, w_keyval, w_output, kv_pool, page_table, selected):
    n_page = lax.axis_size("page")
    n_tensor = lax.axis_size("tensor")
    my_page = lax.axis_index("page")
    my_tensor = lax.axis_index("tensor")
    seqs = selected.shape[1]
    groups = H // KVH
    local_heads = H // n_tensor
    scale = 1.0 / math.sqrt(HD)
    slots = kv_pool.shape[0]
    pool_size = page_table.shape[0]
    device = my_page * n_tensor + my_tensor
    position = float(PAGES * PAGE_TOK)
    seq_share = seqs // n_page
    query_cols = w_query.shape[1]
    sub_heads = w_keyval.shape[1] // HD

    my_slots = device * slots + jnp.arange(slots, dtype=jnp.int32)
    match = page_table[None, :] == my_slots[:, None]
    my_logical = jnp.sum(
        jnp.where(match, jnp.arange(pool_size, dtype=jnp.int32)[None, :], 0), axis=1
    )
    seq_of = my_logical // PAGES
    page_of = my_logical % PAGES
    sel_rows = selected[0][seq_of]
    picked = jnp.any(sel_rows == page_of[:, None, None], axis=2)

    tok_all = gather_blocks(hidden_in[0], "tensor", n_tensor).reshape(seqs, -1)
    part_q = jnp.dot(tok_all, w_query, preferred_element_type=jnp.float32)
    part_kv = jnp.dot(tok_all, w_keyval, preferred_element_type=jnp.float32)
    summed = butterfly_sum(jnp.concatenate([part_q, part_kv], axis=1), "page", n_page)
    query = rotate(summed[:, :query_cols].reshape(seqs, local_heads, HD), position)
    query = query.astype(jnp.bfloat16).reshape(seqs, query_cols)
    keyval = summed[:, query_cols:].reshape(seqs, sub_heads, HD)
    kind_ids = (my_tensor * sub_heads + jnp.arange(sub_heads, dtype=jnp.int32)) % 2
    keyval = jnp.where(kind_ids[None, :, None] == 0, rotate(keyval, position), keyval)
    keyval = keyval.reshape(seqs, -1).astype(jnp.bfloat16)
    new_rows = lax.dynamic_slice_in_dim(keyval, my_page * seq_share, seq_share, 0)

    q_all = gather_blocks(query, "tensor", n_tensor)
    q_all = q_all.reshape(KVH, n_tensor // KVH, seqs, local_heads, HD)
    q_all = q_all.transpose(2, 0, 1, 3, 4).reshape(seqs, KVH, groups, HD)

    loc_acc, loc_total, loc_max = merge_pages(seq_of, picked, q_all, kv_pool)
    loc_acc = loc_acc.reshape(seqs, H, HD)
    loc_total = loc_total[..., 0].reshape(seqs, H)
    loc_max = loc_max[..., 0].reshape(seqs, H)

    blocks = n_page * n_tensor
    def by_owner(x):
        x = x.reshape((n_page, seq_share, n_tensor, local_heads) + x.shape[2:])
        return x.transpose((0, 2, 1, 3) + tuple(range(4, x.ndim))).reshape(blocks, -1)
    rows = seq_share * local_heads
    packed = jnp.concatenate([by_owner(loc_acc), by_owner(loc_total), by_owner(loc_max)], axis=1)
    got = lax.all_to_all(packed, ("page", "tensor"), 0, 0, tiled=True)
    src_acc = got[:, :rows * HD].reshape(blocks, rows, HD)
    src_total = got[:, rows * HD:rows * HD + rows]
    src_max = got[:, rows * HD + rows:]
    top_max = jnp.max(src_max, axis=0)
    rescale = jnp.exp(src_max - top_max[None])
    full_total = jnp.sum(src_total * rescale, axis=0)
    full_acc = jnp.sum(src_acc * rescale[..., None], axis=0)
    heads = (full_acc / full_total[..., None]).astype(jnp.bfloat16)

    heads_all = gather_blocks(heads.reshape(seq_share, local_heads * HD), "page", n_page)
    heads_all = heads_all.reshape(seqs, local_heads * HD)
    part_out = jnp.dot(heads_all, w_output, preferred_element_type=jnp.float32)
    part_out = part_out.reshape(n_tensor, seqs // n_tensor, -1)
    out = jnp.sum(lax.all_to_all(part_out, "tensor", 0, 0, tiled=True), axis=0)
    return (out.astype(jnp.bfloat16)[None], new_rows[None])


def solution(mesh):
    return jax.shard_map(
        per_device,
        mesh=mesh,
        in_specs=(
            P(None, "tensor", "page"),
            P("page", "tensor"),
            P("page", "tensor"),
            P("tensor", "page"),
            P(("page", "tensor"), None, None),
            P(),
            P(),
        ),
        out_specs=(P(None, "tensor", "page"), P(None, "page", "tensor")),
        check_vma=False,
    )
```

```python
import math

import jax
import jax.numpy as jnp
from jax import lax
from jax.experimental import pallas as pl
from jax.experimental.pallas import tpu as pltpu
from jax.sharding import PartitionSpec as P

H = 64
KVH = 8
HD = 128
PAGE_TOK = 64
PAGES = 256


NEG_BIG = -1e30


def frequencies(head_dim):
    half_dim = head_dim // 2
    index = jnp.arange(half_dim, dtype=jnp.float32)
    base_freq = jnp.exp(-(2.0 * index / head_dim) * math.log(500000.0))
    wavelen = 2.0 * math.pi / base_freq
    smooth = (8192.0 / wavelen - 1.0) / 3.0
    middle = (1.0 - smooth) * base_freq / 8.0 + smooth * base_freq
    scaled = jnp.where(wavelen > 8192.0, base_freq / 8.0, base_freq)
    is_middle = jnp.logical_and(wavelen >= 2048.0, wavelen <= 8192.0)
    return jnp.where(is_middle, middle, scaled)


def rotate(vectors, position):
    half_dim = vectors.shape[-1] // 2
    angles = position * frequencies(vectors.shape[-1])
    cosine = jnp.cos(angles)
    sine_v = jnp.sin(angles)
    first_half = vectors[..., :half_dim]
    second_half = vectors[..., half_dim:]
    return jnp.concatenate(
        [first_half * cosine - second_half * sine_v, first_half * sine_v + second_half * cosine],
        axis=-1,
    )


def gather_blocks(x, axis, n):
    return lax.all_to_all(jnp.broadcast_to(x[None], (n,) + x.shape), axis, 0, 0, tiled=True)


def butterfly_sum(x, axis, n):
    d = 1
    while d < n:
        x = x + lax.ppermute(x, axis, [(i, i ^ d) for i in range(n)])
        d *= 2
    return x


DEPTH = 32
UNROLL = 16

def merge_kernel(seq_ref, order_ref, count_ref, q_ref, kv_hbm, acc_ref, stats_ref, tot_ref, max_ref, buf, sems):
    scale = 1.0 / math.sqrt(HD)
    acc_ref[...] = jnp.zeros(acc_ref.shape, jnp.float32)
    tot_ref[...] = jnp.zeros(tot_ref.shape, jnp.float32)
    max_ref[...] = jnp.full(max_ref.shape, NEG_BIG, jnp.float32)

    count = count_ref[0]
    padded = (count + UNROLL - 1) // UNROLL * UNROLL

    def copy_of(k):
        e = order_ref[k]
        slot = e // KVH
        g = e % KVH
        return pltpu.make_async_copy(
            kv_hbm.at[slot, :, pl.ds(g * 2 * HD, 2 * HD)], buf.at[k % DEPTH], sems.at[k % DEPTH]
        )

    for k in range(DEPTH):
        @pl.when(k < padded)
        def _start():
            copy_of(k).start()

    rows = lax.broadcasted_iota(jnp.int32, (UNROLL * 8, UNROLL * 64), 0) // 8
    cols = lax.broadcasted_iota(jnp.int32, (UNROLL * 8, UNROLL * 64), 1) // 64
    own_page = rows == cols

    def attend_all(ks):
        where = []
        qs, keys, vals = [], [], []
        for k in ks:
            e = order_ref[k]
            g = e % KVH
            seq = seq_ref[e // KVH]
            page = buf[k % DEPTH]
            where.append((seq, g))
            qs.append(q_ref[seq, g])
            keys.append(page[:, :HD])
            vals.append(page[:, HD:])
        sc = lax.dot_general(jnp.concatenate(qs, axis=0), jnp.concatenate(keys, axis=0),
                             (((1,), (1,)), ((), ())), preferred_element_type=jnp.float32) * scale
        sc = jnp.where(own_page, sc, -jnp.inf)
        pm = jnp.max(sc, axis=1, keepdims=True)
        wt = jnp.exp(sc - pm).astype(jnp.bfloat16)
        pt = jnp.sum(wt.astype(jnp.float32), axis=1, keepdims=True)
        pa = jnp.dot(wt, jnp.concatenate(vals, axis=0), preferred_element_type=jnp.float32)
        rows8 = [slice(8 * u, 8 * u + 8) for u in range(len(ks))]
        return [(seq, g, pm[r], pt[r], pa[r]) for (seq, g), r in zip(where, rows8)]

    def update(seq, g, pm, pt, pa, live):
        m_old = max_ref[seq, g]
        m_new = jnp.where(live, jnp.maximum(m_old, pm), m_old)
        alpha = jnp.exp(m_old - m_new)
        beta = jnp.where(live, jnp.exp(pm - m_new), 0.0)
        acc_ref[seq, g] = acc_ref[seq, g] * alpha + pa * beta
        tot_ref[seq, g] = tot_ref[seq, g] * alpha + pt * beta
        max_ref[seq, g] = m_new

    def body(step, carry):
        ks = [step * UNROLL + u for u in range(UNROLL)]
        for k in ks:
            copy_of(k).wait()
        done = attend_all(ks)
        for k, res in zip(ks, done):
            update(*res, k < count)
        for k in ks:
            @pl.when(k + DEPTH < padded)
            def _next():
                copy_of(k + DEPTH).start()
        return carry

    lax.fori_loop(0, padded // UNROLL, body, 0)

    heads = KVH * (H // KVH)
    diag = (lax.broadcasted_iota(jnp.int32, (heads, 128), 0)
            == lax.broadcasted_iota(jnp.int32, (heads, 128), 1))

    def emit(s, carry):
        for i, ref in enumerate((tot_ref, max_ref)):
            col = ref[s].reshape(heads, 128)
            stats_ref[i, s] = jnp.sum(jnp.where(diag, col, 0.0), axis=0, keepdims=True)[:, :heads]
        return carry

    lax.fori_loop(0, stats_ref.shape[1], emit, 0)


def merge_pages(seq_of, picked, q_all, kv):
    slots, tok, width = kv.shape
    seqs = q_all.shape[0]
    full = (seqs, KVH, H // KVH, HD)
    flags = picked.reshape(-1).astype(jnp.int32)
    pairs = flags.shape[0]
    place = jnp.cumsum(flags) - 1
    hit = (place[None, :] == jnp.arange(pairs, dtype=jnp.int32)[:, None]) & (flags[None, :] == 1)
    order = jnp.sum(jnp.where(hit, jnp.arange(pairs, dtype=jnp.int32)[None, :], 0), axis=1)
    count = jnp.sum(flags, keepdims=True)
    vmem = pl.BlockSpec(memory_space=pltpu.VMEM)
    smem = pl.BlockSpec(memory_space=pltpu.SMEM)
    return pl.pallas_call(
        merge_kernel,
        in_specs=[smem, smem, smem, vmem, pl.BlockSpec(memory_space=pl.ANY)],
        out_specs=[vmem] * 2,
        out_shape=[jax.ShapeDtypeStruct(full, jnp.float32),
                   jax.ShapeDtypeStruct((2, seqs, 1, H), jnp.float32)],
        scratch_shapes=[
            pltpu.VMEM(full, jnp.float32),
            pltpu.VMEM(full, jnp.float32),
            pltpu.VMEM((DEPTH, tok, 2 * HD), kv.dtype),
            pltpu.SemaphoreType.DMA((DEPTH,)),
        ],
    )(seq_of, order, count, q_all, kv)


def per_device(hidden_in, w_query, w_keyval, w_output, kv_pool, page_table, selected):
    n_page = lax.axis_size("page")
    n_tensor = lax.axis_size("tensor")
    my_page = lax.axis_index("page")
    my_tensor = lax.axis_index("tensor")
    seqs = selected.shape[1]
    groups = H // KVH
    local_heads = H // n_tensor
    scale = 1.0 / math.sqrt(HD)
    slots = kv_pool.shape[0]
    pool_size = page_table.shape[0]
    device = my_page * n_tensor + my_tensor
    position = float(PAGES * PAGE_TOK)
    seq_share = seqs // n_page
    query_cols = w_query.shape[1]
    sub_heads = w_keyval.shape[1] // HD

    my_slots = device * slots + jnp.arange(slots, dtype=jnp.int32)
    match = page_table[None, :] == my_slots[:, None]
    my_logical = jnp.sum(
        jnp.where(match, jnp.arange(pool_size, dtype=jnp.int32)[None, :], 0), axis=1
    )
    seq_of = my_logical // PAGES
    page_of = my_logical % PAGES
    sel_rows = selected[0][seq_of]
    picked = jnp.any(sel_rows == page_of[:, None, None], axis=2)

    tok_all = gather_blocks(hidden_in[0], "tensor", n_tensor).reshape(seqs, -1)
    part_q = jnp.dot(tok_all, w_query, preferred_element_type=jnp.float32)
    part_kv = jnp.dot(tok_all, w_keyval, preferred_element_type=jnp.float32)
    summed = butterfly_sum(jnp.concatenate([part_q, part_kv], axis=1), "page", n_page)
    query = rotate(summed[:, :query_cols].reshape(seqs, local_heads, HD), position)
    query = query.astype(jnp.bfloat16).reshape(seqs, query_cols)
    keyval = summed[:, query_cols:].reshape(seqs, sub_heads, HD)
    kind_ids = (my_tensor * sub_heads + jnp.arange(sub_heads, dtype=jnp.int32)) % 2
    keyval = jnp.where(kind_ids[None, :, None] == 0, rotate(keyval, position), keyval)
    keyval = keyval.reshape(seqs, -1).astype(jnp.bfloat16)
    new_rows = lax.dynamic_slice_in_dim(keyval, my_page * seq_share, seq_share, 0)

    q_all = gather_blocks(query, "tensor", n_tensor)
    q_all = q_all.reshape(KVH, n_tensor // KVH, seqs, local_heads, HD)
    q_all = q_all.transpose(2, 0, 1, 3, 4).reshape(seqs, KVH, groups, HD)

    loc_acc, stats = merge_pages(seq_of, picked, q_all, kv_pool)
    loc_acc = loc_acc.reshape(seqs, H, HD)
    loc_total = stats[0].reshape(seqs, H)
    loc_max = stats[1].reshape(seqs, H)

    blocks = n_page * n_tensor
    def by_owner(x):
        x = x.reshape((n_page, seq_share, n_tensor, local_heads) + x.shape[2:])
        return x.transpose((0, 2, 1, 3) + tuple(range(4, x.ndim))).reshape(blocks, -1)
    rows = seq_share * local_heads
    packed = jnp.concatenate([by_owner(loc_acc), by_owner(loc_total), by_owner(loc_max)], axis=1)
    got = lax.all_to_all(packed, ("page", "tensor"), 0, 0, tiled=True)
    src_acc = got[:, :rows * HD].reshape(blocks, rows, HD)
    src_total = got[:, rows * HD:rows * HD + rows]
    src_max = got[:, rows * HD + rows:]
    top_max = jnp.max(src_max, axis=0)
    rescale = jnp.exp(src_max - top_max[None])
    full_total = jnp.sum(src_total * rescale, axis=0)
    full_acc = jnp.sum(src_acc * rescale[..., None], axis=0)
    heads = (full_acc / full_total[..., None]).astype(jnp.bfloat16)

    heads_all = gather_blocks(heads.reshape(seq_share, local_heads * HD), "page", n_page)
    heads_all = heads_all.reshape(seqs, local_heads * HD)
    part_out = jnp.dot(heads_all, w_output, preferred_element_type=jnp.float32)
    part_out = part_out.reshape(n_tensor, seqs // n_tensor, -1)
    out = jnp.sum(lax.all_to_all(part_out, "tensor", 0, 0, tiled=True), axis=0)
    return (out.astype(jnp.bfloat16)[None], new_rows[None])


def solution(mesh):
    return jax.shard_map(
        per_device,
        mesh=mesh,
        in_specs=(
            P(None, "tensor", "page"),
            P("page", "tensor"),
            P("page", "tensor"),
            P("tensor", "page"),
            P(("page", "tensor"), None, None),
            P(),
            P(),
        ),
        out_specs=(P(None, "tensor", "page"), P(None, "page", "tensor")),
        check_vma=False,
    )
```

```python
import math

import jax
import jax.numpy as jnp
from jax import lax
from jax.experimental import pallas as pl
from jax.experimental.pallas import tpu as pltpu
from jax.sharding import PartitionSpec as P

H = 64
KVH = 8
HD = 128
PAGE_TOK = 64
PAGES = 256


NEG_BIG = -1e30


def frequencies(head_dim):
    half_dim = head_dim // 2
    index = jnp.arange(half_dim, dtype=jnp.float32)
    base_freq = jnp.exp(-(2.0 * index / head_dim) * math.log(500000.0))
    wavelen = 2.0 * math.pi / base_freq
    smooth = (8192.0 / wavelen - 1.0) / 3.0
    middle = (1.0 - smooth) * base_freq / 8.0 + smooth * base_freq
    scaled = jnp.where(wavelen > 8192.0, base_freq / 8.0, base_freq)
    is_middle = jnp.logical_and(wavelen >= 2048.0, wavelen <= 8192.0)
    return jnp.where(is_middle, middle, scaled)


def rotate(vectors, position):
    half_dim = vectors.shape[-1] // 2
    angles = position * frequencies(vectors.shape[-1])
    cosine = jnp.cos(angles)
    sine_v = jnp.sin(angles)
    first_half = vectors[..., :half_dim]
    second_half = vectors[..., half_dim:]
    return jnp.concatenate(
        [first_half * cosine - second_half * sine_v, first_half * sine_v + second_half * cosine],
        axis=-1,
    )


def gather_blocks(x, axis, n):
    return lax.all_to_all(jnp.broadcast_to(x[None], (n,) + x.shape), axis, 0, 0, tiled=True)


def butterfly_sum(x, axis, n):
    d = 1
    while d < n:
        x = x + lax.ppermute(x, axis, [(i, i ^ d) for i in range(n)])
        d *= 2
    return x


DEPTH = 32
UNROLL = 16

def merge_kernel(seq_ref, order_ref, count_ref, q_ref, kv_hbm, acc_ref, stats_ref, tot_ref, max_ref, buf, sems):
    scale = 1.0 / math.sqrt(HD)
    acc_ref[...] = jnp.zeros(acc_ref.shape, jnp.float32)
    tot_ref[...] = jnp.zeros(tot_ref.shape, jnp.float32)
    max_ref[...] = jnp.full(max_ref.shape, NEG_BIG, jnp.float32)

    count = count_ref[0]
    padded = (count + UNROLL - 1) // UNROLL * UNROLL

    def copy_of(k):
        e = order_ref[k]
        slot = e // KVH
        g = e % KVH
        return pltpu.make_async_copy(
            kv_hbm.at[slot, :, pl.ds(g * 2 * HD, 2 * HD)], buf.at[k % DEPTH], sems.at[k % DEPTH]
        )

    for k in range(DEPTH):
        @pl.when(k < padded)
        def _start():
            copy_of(k).start()

    rows = lax.broadcasted_iota(jnp.int32, (UNROLL * 8, UNROLL * 64), 0) // 8
    cols = lax.broadcasted_iota(jnp.int32, (UNROLL * 8, UNROLL * 64), 1) // 64
    own_page = rows == cols

    def attend_all(ks):
        where = []
        qs, keys, vals = [], [], []
        for k in ks:
            e = order_ref[k]
            g = e % KVH
            seq = seq_ref[e // KVH]
            page = buf[k % DEPTH]
            where.append((seq, g))
            qs.append(q_ref[seq, g])
            keys.append(page[:, :HD])
            vals.append(page[:, HD:])
        sc = lax.dot_general(jnp.concatenate(qs, axis=0), jnp.concatenate(keys, axis=0),
                             (((1,), (1,)), ((), ())), preferred_element_type=jnp.float32) * scale
        sc = jnp.where(own_page, sc, -jnp.inf)
        pm = jnp.max(sc, axis=1, keepdims=True)
        wt = jnp.exp(sc - pm).astype(jnp.bfloat16)
        pt = jnp.sum(wt.astype(jnp.float32), axis=1, keepdims=True)
        pa = jnp.dot(wt, jnp.concatenate(vals, axis=0), preferred_element_type=jnp.float32)
        rows8 = [slice(8 * u, 8 * u + 8) for u in range(len(ks))]
        return [(seq, g, pm[r], pt[r], pa[r]) for (seq, g), r in zip(where, rows8)]

    def update(seq, g, pm, pt, pa, live):
        m_old = max_ref[seq, g]
        m_new = jnp.where(live, jnp.maximum(m_old, pm), m_old)
        alpha = jnp.exp(m_old - m_new)
        beta = jnp.where(live, jnp.exp(pm - m_new), 0.0)
        acc_ref[seq, g] = acc_ref[seq, g] * alpha + pa * beta
        tot_ref[seq, g] = tot_ref[seq, g] * alpha + pt * beta
        max_ref[seq, g] = m_new

    def body(step, carry):
        ks = [step * UNROLL + u for u in range(UNROLL)]
        for k in ks:
            copy_of(k).wait()
        done = attend_all(ks)
        for k, res in zip(ks, done):
            update(*res, k < count)
        for k in ks:
            @pl.when(k + DEPTH < padded)
            def _next():
                copy_of(k + DEPTH).start()
        return carry

    lax.fori_loop(0, padded // UNROLL, body, 0)

    heads = KVH * (H // KVH)
    diag = (lax.broadcasted_iota(jnp.int32, (heads, 128), 0)
            == lax.broadcasted_iota(jnp.int32, (heads, 128), 1))

    def emit(s, carry):
        for i, ref in enumerate((tot_ref, max_ref)):
            col = ref[s].reshape(heads, 128)
            stats_ref[i, s] = jnp.sum(jnp.where(diag, col, 0.0), axis=0, keepdims=True)[:, :heads]
        return carry

    lax.fori_loop(0, stats_ref.shape[1], emit, 0)


def merge_pages(seq_of, picked, q_all, kv):
    slots, tok, width = kv.shape
    seqs = q_all.shape[0]
    full = (seqs, KVH, H // KVH, HD)
    flags = picked.reshape(-1).astype(jnp.int32)
    pairs = flags.shape[0]
    place = jnp.cumsum(flags) - 1
    hit = (place[None, :] == jnp.arange(pairs, dtype=jnp.int32)[:, None]) & (flags[None, :] == 1)
    order = jnp.sum(jnp.where(hit, jnp.arange(pairs, dtype=jnp.int32)[None, :], 0), axis=1)
    count = jnp.sum(flags, keepdims=True)
    vmem = pl.BlockSpec(memory_space=pltpu.VMEM)
    smem = pl.BlockSpec(memory_space=pltpu.SMEM)
    return pl.pallas_call(
        merge_kernel,
        in_specs=[smem, smem, smem, vmem, pl.BlockSpec(memory_space=pl.ANY)],
        out_specs=[vmem] * 2,
        out_shape=[jax.ShapeDtypeStruct(full, jnp.float32),
                   jax.ShapeDtypeStruct((2, seqs, 1, H), jnp.float32)],
        scratch_shapes=[
            pltpu.VMEM(full, jnp.float32),
            pltpu.VMEM(full, jnp.float32),
            pltpu.VMEM((DEPTH, tok, 2 * HD), kv.dtype),
            pltpu.SemaphoreType.DMA((DEPTH,)),
        ],
    )(seq_of, order, count, q_all, kv)


def per_device(hidden_in, w_query, w_keyval, w_output, kv_pool, page_table, selected):
    n_page = lax.axis_size("page")
    n_tensor = lax.axis_size("tensor")
    my_page = lax.axis_index("page")
    my_tensor = lax.axis_index("tensor")
    seqs = selected.shape[1]
    groups = H // KVH
    local_heads = H // n_tensor
    scale = 1.0 / math.sqrt(HD)
    slots = kv_pool.shape[0]
    pool_size = page_table.shape[0]
    device = my_page * n_tensor + my_tensor
    position = float(PAGES * PAGE_TOK)
    seq_share = seqs // n_page
    query_cols = w_query.shape[1]
    sub_heads = w_keyval.shape[1] // HD

    my_slots = device * slots + jnp.arange(slots, dtype=jnp.int32)
    match = page_table[None, :] == my_slots[:, None]
    my_logical = jnp.sum(
        jnp.where(match, jnp.arange(pool_size, dtype=jnp.int32)[None, :], 0), axis=1
    )
    seq_of = my_logical // PAGES
    page_of = my_logical % PAGES
    sel_rows = selected[0][seq_of]
    picked = jnp.any(sel_rows == page_of[:, None, None], axis=2)

    tok_all = gather_blocks(hidden_in[0], "tensor", n_tensor).reshape(seqs, -1)
    part_q = jnp.dot(tok_all, w_query, preferred_element_type=jnp.float32)
    part_kv = jnp.dot(tok_all, w_keyval, preferred_element_type=jnp.float32)
    summed = butterfly_sum(jnp.concatenate([part_q, part_kv], axis=1), "page", n_page)
    query = rotate(summed[:, :query_cols].reshape(seqs, local_heads, HD), position)
    query = query.astype(jnp.bfloat16).reshape(seqs, query_cols)
    keyval = summed[:, query_cols:].reshape(seqs, sub_heads, HD)
    kind_ids = (my_tensor * sub_heads + jnp.arange(sub_heads, dtype=jnp.int32)) % 2
    keyval = jnp.where(kind_ids[None, :, None] == 0, rotate(keyval, position), keyval)
    keyval = keyval.reshape(seqs, -1).astype(jnp.bfloat16)
    new_rows = lax.dynamic_slice_in_dim(keyval, my_page * seq_share, seq_share, 0)

    q_all = gather_blocks(query, "tensor", n_tensor)
    q_all = q_all.reshape(KVH, n_tensor // KVH, seqs, local_heads, HD)
    q_all = q_all.transpose(2, 0, 1, 3, 4).reshape(seqs, KVH, groups, HD)

    loc_acc, stats = merge_pages(seq_of, picked, q_all, kv_pool)
    loc_acc = loc_acc.reshape(seqs, H, HD)
    loc_total = stats[0].reshape(seqs, H)
    loc_max = stats[1].reshape(seqs, H)

    blocks = n_page * n_tensor
    def by_owner(x):
        x = x.reshape((n_page, seq_share, n_tensor, local_heads) + x.shape[2:])
        return x.transpose((0, 2, 1, 3) + tuple(range(4, x.ndim))).reshape(blocks, -1)
    rows = seq_share * local_heads
    to_bf16 = lambda x: lax.reduce_precision(x, exponent_bits=8, mantissa_bits=7)
    hi = to_bf16(loc_max)
    rest = loc_max - hi
    mid = to_bf16(rest)
    max_hi = hi.astype(jnp.bfloat16)
    max_mid = mid.astype(jnp.bfloat16)
    max_lo = to_bf16(rest - mid).astype(jnp.bfloat16)
    packed = jnp.concatenate(
        [
            by_owner(loc_acc.astype(jnp.bfloat16)),
            by_owner(loc_total.astype(jnp.bfloat16)),
            by_owner(max_hi),
            by_owner(max_mid),
            by_owner(max_lo),
        ],
        axis=1,
    )
    got = lax.all_to_all(packed, ("page", "tensor"), 0, 0, tiled=True).astype(jnp.float32)
    base = rows * HD
    src_acc = got[:, :base].reshape(blocks, rows, HD)
    src_total = got[:, base:base + rows]
    src_max = (got[:, base + rows:base + 2 * rows] + got[:, base + 2 * rows:base + 3 * rows]) + got[:, base + 3 * rows:]
    top_max = jnp.max(src_max, axis=0)
    rescale = jnp.exp(src_max - top_max[None])
    full_total = jnp.sum(src_total * rescale, axis=0)
    full_acc = jnp.sum(src_acc * rescale[..., None], axis=0)
    heads = (full_acc / full_total[..., None]).astype(jnp.bfloat16)

    heads_all = gather_blocks(heads.reshape(seq_share, local_heads * HD), "page", n_page)
    heads_all = heads_all.reshape(seqs, local_heads * HD)
    part_out = jnp.dot(heads_all, w_output, preferred_element_type=jnp.float32)
    part_out = part_out.reshape(n_tensor, seqs // n_tensor, -1)
    out = jnp.sum(lax.all_to_all(part_out, "tensor", 0, 0, tiled=True), axis=0)
    return (out.astype(jnp.bfloat16)[None], new_rows[None])


def solution(mesh):
    return jax.shard_map(
        per_device,
        mesh=mesh,
        in_specs=(
            P(None, "tensor", "page"),
            P("page", "tensor"),
            P("page", "tensor"),
            P("tensor", "page"),
            P(("page", "tensor"), None, None),
            P(),
            P(),
        ),
        out_specs=(P(None, "tensor", "page"), P(None, "page", "tensor")),
        check_vma=False,
    )
```
